256 devices in a mesh: walker: 2 (over core), elec: 128 (over x, z, y).
Axes of the slice: x: 4, y: 4, z: 8, core: 2. Of those that a mesh axis runs over, the one named last changes fastest.
Arguments:
- inverse_rows: float32 [16384, 8192], P(('walker', 'elec')), parts along dimension 0
- row_values: float32 [128, 8, 64], P('walker'), parts along dimension 0
- orbital_blocks: int32 [128, 8], P('walker'), parts along dimension 0, may hold values from 0 to 127, as said below
- moved: int32 [128], P('walker'), parts along dimension 0, may hold values from 0 to 8191
- accepted: int32 [128], P('walker'), parts along dimension 0, may hold values 0 or 1
Outputs:
- new_inverse: float32 [16384, 8192], P(('walker', 'elec')), parts along dimension 0
- ratios: float32 [128], P('walker'), parts along dimension 0
The draws below stay inside these ranges and needn't reach their ends.
There are 2 independent parts, one for each index of `walker`. The reference program is written for one: setup_inputs(seed, part) draws one part's arguments, and reference() takes and returns one part's arrays. A program takes and returns all parts, laid end to end along the dimension named above; each array names one. Nothing has to cross between parts.
Inputs may be any that keep to these rules, and one draw needn't show every extreme that they name: `orbital_blocks`: the 8 blocks of a move are distinct, and the first is the block holding orbital number moved[k].
All inputs are finite; a program needn't handle non-finite values.
Results may differ from the reference program's by a relative error of at most 0.0001.
Values sent between devices are 32-bit elements; how exact they have to be, the bound alone decides.
No kernel may reach another device: no remote copies, remote signals or barrier semaphores. Data moves between devices by JAX's collectives and lax.ppermute only.
A program may use at most 64 MiB of HBM per device.

```python
import math
import jax
import jax.numpy as jnp
from jax import lax

NORB = 8192
BLK = 64
MOVES = 64
NZ_BLOCKS = 8


def moved_helper(key):
    return jax.random.randint(jax.random.fold_in(key, 11), (MOVES,), 0, NORB, dtype=jnp.int32)


def draw_moved(key, part):
    return moved_helper(key)


def draw_orbital_blocks(key, part):
    moved_ids = moved_helper(key)
    block_count = NORB // BLK
    home_block = moved_ids // BLK
    row_keys = jax.random.split(jax.random.fold_in(key, 23), MOVES)
    others = jax.vmap(lambda row_key: jax.random.permutation(row_key, block_count - 1)[:NZ_BLOCKS - 1])(row_keys)
    rest = (home_block[:, None] + 1 + others.astype(jnp.int32)) % block_count
    return jnp.concatenate([home_block[:, None], rest], axis=1).astype(jnp.int32)


def draw_row_values(key, part):
    moved_ids = moved_helper(key)
    noise_key = jax.random.fold_in(key, 37)
    noise = 0.1 * jax.random.normal(noise_key, (MOVES, NZ_BLOCKS, BLK), jnp.float32)
    home_value = jax.random.uniform(jax.random.fold_in(key, 41), (MOVES,), jnp.float32, 0.6, 1.0)
    first_slot = jnp.arange(NZ_BLOCKS)[None, :, None] == 0
    spot = first_slot & (jnp.arange(BLK)[None, None, :] == (moved_ids % BLK)[:, None, None])
    return (noise + jnp.where(spot, home_value[:, None, None], 0.0)).astype(jnp.float32)


def draw_inverse_rows(key, part):
    noise_key = jax.random.fold_in(key, 53)
    scale = 2.0 / math.sqrt(NORB)
    noise = jax.random.normal(noise_key, (NORB, NORB), jnp.float32)
    index = jnp.arange(NORB)
    diagonal = (index[:, None] == index[None, :]).astype(jnp.float32)
    return (scale * noise + diagonal).astype(jnp.float32)


def place_ends(entries, rng, low, high):
    dims = entries.shape
    place = [jax.random.randint(jax.random.fold_in(rng, axis), (), 0, dims[axis]) for axis in range(len(dims))]
    entries = entries.at[tuple(place)].set(low)
    longest = dims.index(max(dims))
    place[longest] = (place[longest] + 1) % dims[longest]
    return entries.at[tuple(place)].set(high)


def setup_inputs(seed: int = 0, part: int = 0) -> dict:
    key_of = jax.random.split(jax.random.key(seed), 6)
    part_keys = jax.random.split(jax.random.fold_in(key_of[5], part), 6)
    return {
        "inverse_rows": draw_inverse_rows(jax.random.fold_in(jax.random.fold_in(key_of[5], part), 71), part),
        "row_values": draw_row_values(jax.random.fold_in(jax.random.fold_in(key_of[5], part), 71), part),
        "orbital_blocks": draw_orbital_blocks(jax.random.fold_in(jax.random.fold_in(key_of[5], part), 71), part),
        "moved": draw_moved(jax.random.fold_in(jax.random.fold_in(key_of[5], part), 71), part),
        "accepted": place_ends((jax.random.randint(part_keys[4], (MOVES,), 0, 3) < 2).astype(jnp.int32), jax.random.fold_in(part_keys[4], 1), 0, 1),
    }


HI = lax.Precision.HIGHEST


def dense_change(row_values, orbital_blocks):
    block_count = NORB // BLK
    onehot = (orbital_blocks[:, :, None] == jnp.arange(block_count, dtype=jnp.int32)[None, None, :]).astype(jnp.float32)
    dense = jnp.einsum("ksb,kst->kbt", onehot, row_values.astype(jnp.float32), precision=HI)
    return dense.reshape(MOVES, NORB)


def border_step(coupling, row_vec, col_vec, accept_flag, unit_row):
    left_vec = jnp.dot(row_vec, coupling, precision=HI)
    right_vec = jnp.dot(coupling, col_vec, precision=HI)
    det_ratio = 1.0 + jnp.dot(row_vec, unit_row, precision=HI) - jnp.dot(left_vec, col_vec, precision=HI)
    coupling = coupling + accept_flag * jnp.outer(right_vec - unit_row, left_vec - unit_row) / det_ratio
    return coupling, det_ratio


def run_border(intersection, accepted):
    def one_step(coupling, step_items):
        row_vec, col_vec, accept_flag, unit_row = step_items
        return border_step(coupling, row_vec, col_vec, accept_flag, unit_row)

    start_value = jnp.zeros((MOVES, MOVES), jnp.float32)
    step_items = (intersection, intersection.T, accepted.astype(jnp.float32), jnp.eye(MOVES, dtype=jnp.float32))
    return lax.scan(one_step, start_value, step_items)


def reference(inverse_rows, row_values, orbital_blocks, moved, accepted):
    change = dense_change(row_values, orbital_blocks)
    weights = jnp.dot(change, inverse_rows, precision=HI)
    intersection = jnp.take(weights, moved.astype(jnp.int32), axis=1)
    coupling, ratios = run_border(intersection, accepted)
    picked = jnp.take(inverse_rows, moved.astype(jnp.int32), axis=1)
    factor = jnp.dot(picked, coupling, precision=HI)
    new_inverse = inverse_rows - jnp.dot(factor, weights, precision=HI)
    return new_inverse, ratios
```

```python
import jax
import jax.numpy as jnp
from jax import lax
from jax.sharding import PartitionSpec as P

MOVES = 64


HI = lax.Precision.HIGHEST


def border_step(coupling, row_vec, col_vec, accept_flag, unit_row):
    left_vec = jnp.dot(row_vec, coupling, precision=HI)
    right_vec = jnp.dot(coupling, col_vec, precision=HI)
    det_ratio = (
        1.0 + jnp.dot(row_vec, unit_row, precision=HI) - jnp.dot(left_vec, col_vec, precision=HI)
    )
    coupling = (
        coupling + accept_flag * jnp.outer(right_vec - unit_row, left_vec - unit_row) / det_ratio
    )
    return (coupling, det_ratio)


def run_border(intersection, accepted):

    def one_step(coupling, step_items):
        row_vec, col_vec, accept_flag, unit_row = step_items
        return border_step(coupling, row_vec, col_vec, accept_flag, unit_row)

    start_value = jnp.zeros((MOVES, MOVES), jnp.float32)
    step_items = (
        intersection,
        intersection.T,
        accepted.astype(jnp.float32),
        jnp.eye(MOVES, dtype=jnp.float32),
    )
    return lax.scan(one_step, start_value, step_items)


def on_device(inverse_rows, row_values, orbital_blocks, moved, accepted):
    row_count = inverse_rows.shape[0]
    block_width = row_values.shape[2]
    blocks_here = row_count // block_width
    owned_blocks = lax.axis_index("elec") * blocks_here + jnp.arange(blocks_here, dtype=jnp.int32)
    onehot = (orbital_blocks[:, :, None] == owned_blocks[None, None, :]).astype(jnp.float32)
    change = jnp.einsum("ksb,kst->kbt", onehot, row_values, precision=HI).reshape(MOVES, row_count)
    picked = jnp.take(inverse_rows, moved, axis=1)
    local_weights = jnp.dot(change, inverse_rows, precision=HI)
    full_weights = lax.psum(local_weights, "elec")
    intersection = jnp.take(full_weights, moved, axis=1)
    coupling, ratios = run_border(intersection, accepted)
    factor = jnp.dot(picked, coupling, precision=HI)
    new_inverse = inverse_rows - jnp.dot(factor, full_weights, precision=HI)
    return (new_inverse, ratios)


def solution(mesh):
    placed = (
        P(("walker", "elec"), None),
        P("walker", None, None),
        P("walker", None),
        P("walker"),
        P("walker"),
    )
    return jax.shard_map(
        on_device,
        mesh=mesh,
        in_specs=placed,
        out_specs=(P(("walker", "elec"), None), P("walker")),
        check_vma=False,
    )
```

```python
import jax
import jax.numpy as jnp
from jax import lax
from jax.sharding import PartitionSpec as P
from jax.experimental import pallas as pl
from jax.experimental.pallas import tpu as pltpu

MOVES = 64


HI = lax.Precision.HIGHEST


def border_step(coupling, row_vec, col_vec, accept_flag, unit_row):
    left_vec = jnp.dot(row_vec, coupling, precision=HI)
    right_vec = jnp.dot(coupling, col_vec, precision=HI)
    det_ratio = (
        1.0 + jnp.dot(row_vec, unit_row, precision=HI) - jnp.dot(left_vec, col_vec, precision=HI)
    )
    coupling = (
        coupling + accept_flag * jnp.outer(right_vec - unit_row, left_vec - unit_row) / det_ratio
    )
    return (coupling, det_ratio)


def run_border(intersection, accepted):

    def one_step(coupling, step_items):
        row_vec, col_vec, accept_flag, unit_row = step_items
        return border_step(coupling, row_vec, col_vec, accept_flag, unit_row)

    start_value = jnp.zeros((MOVES, MOVES), jnp.float32)
    step_items = (
        intersection,
        intersection.T,
        accepted.astype(jnp.float32),
        jnp.eye(MOVES, dtype=jnp.float32),
    )
    return lax.scan(one_step, start_value, step_items)


def _border_kernel(m_ref, mt_ref, acc_ref, c_ref, r_ref):
    n = m_ref.shape[0]
    lane = lax.broadcasted_iota(jnp.int32, (1, n), 1)
    sub = lax.broadcasted_iota(jnp.int32, (n, 1), 0)
    mt = mt_ref[...]
    acc = acc_ref[...]

    def step(k, carry):
        c, ratios = carry
        e_row = (lane == k).astype(jnp.float32)
        e_col = (sub == k).astype(jnp.float32)
        row_row = m_ref[pl.ds(k, 1), :]
        col_row = mt_ref[pl.ds(k, 1), :]
        row_col = jnp.sum(mt * e_row, axis=1, keepdims=True)
        left = jnp.sum(c * row_col, axis=0, keepdims=True)
        right = jnp.sum(c * col_row, axis=1, keepdims=True)
        diag = jnp.sum(row_row * e_row, axis=1, keepdims=True)
        lc = jnp.sum(left * col_row, axis=1, keepdims=True)
        ratio = 1.0 + diag - lc
        flag = jnp.sum(acc * e_row, axis=1, keepdims=True)
        c = c + flag * ((right - e_col) * (left - e_row)) / ratio
        ratios = ratios + e_row * ratio
        return c, ratios

    c0 = jnp.zeros((n, n), jnp.float32)
    r0 = jnp.zeros((1, n), jnp.float32)
    c, ratios = lax.fori_loop(0, n, step, (c0, r0))
    c_ref[...] = c
    r_ref[...] = ratios


def border(intersection, accepted):
    n = intersection.shape[0]
    vm = pl.BlockSpec(memory_space=pltpu.VMEM)
    c, r = pl.pallas_call(
        _border_kernel,
        out_shape=(jax.ShapeDtypeStruct((n, n), jnp.float32), jax.ShapeDtypeStruct((1, n), jnp.float32)),
        in_specs=[vm, vm, vm],
        out_specs=(vm, vm),
    )(intersection, intersection.T, accepted.astype(jnp.float32).reshape(1, n))
    return c, r.reshape(n)


def on_device(inverse_rows, row_values, orbital_blocks, moved, accepted):
    row_count = inverse_rows.shape[0]
    block_width = row_values.shape[2]
    blocks_here = row_count // block_width
    owned_blocks = lax.axis_index("elec") * blocks_here + jnp.arange(blocks_here, dtype=jnp.int32)
    onehot = (orbital_blocks[:, :, None] == owned_blocks[None, None, :]).astype(jnp.float32)
    change = jnp.einsum("ksb,kst->kbt", onehot, row_values, precision=HI).reshape(MOVES, row_count)
    picked = jnp.take(inverse_rows, moved, axis=1)
    local_weights = jnp.dot(change, inverse_rows, precision=HI)
    full_weights = lax.psum(local_weights, "elec")
    intersection = jnp.take(full_weights, moved, axis=1)
    coupling, ratios = border(intersection, accepted)
    factor = jnp.dot(picked, coupling, precision=HI)
    new_inverse = inverse_rows - jnp.dot(factor, full_weights, precision=HI)
    return (new_inverse, ratios)


def solution(mesh):
    placed = (
        P(("walker", "elec"), None),
        P("walker", None, None),
        P("walker", None),
        P("walker"),
        P("walker"),
    )
    return jax.shard_map(
        on_device,
        mesh=mesh,
        in_specs=placed,
        out_specs=(P(("walker", "elec"), None), P("walker")),
        check_vma=False,
    )
```

```python
import jax
import jax.numpy as jnp
from jax import lax
from jax.sharding import Mesh, PartitionSpec as P
from jax.experimental import pallas as pl
from jax.experimental.pallas import tpu as pltpu

MOVES = 64


HI = lax.Precision.HIGHEST


def border_step(coupling, row_vec, col_vec, accept_flag, unit_row):
    left_vec = jnp.dot(row_vec, coupling, precision=HI)
    right_vec = jnp.dot(coupling, col_vec, precision=HI)
    det_ratio = (
        1.0 + jnp.dot(row_vec, unit_row, precision=HI) - jnp.dot(left_vec, col_vec, precision=HI)
    )
    coupling = (
        coupling + accept_flag * jnp.outer(right_vec - unit_row, left_vec - unit_row) / det_ratio
    )
    return (coupling, det_ratio)


def run_border(intersection, accepted):

    def one_step(coupling, step_items):
        row_vec, col_vec, accept_flag, unit_row = step_items
        return border_step(coupling, row_vec, col_vec, accept_flag, unit_row)

    start_value = jnp.zeros((MOVES, MOVES), jnp.float32)
    step_items = (
        intersection,
        intersection.T,
        accepted.astype(jnp.float32),
        jnp.eye(MOVES, dtype=jnp.float32),
    )
    return lax.scan(one_step, start_value, step_items)


def _border_kernel(m_ref, mt_ref, acc_ref, c_ref, r_ref):
    n = m_ref.shape[0]
    lane = lax.broadcasted_iota(jnp.int32, (1, n), 1)
    sub = lax.broadcasted_iota(jnp.int32, (n, 1), 0)
    mt = mt_ref[...]
    acc = acc_ref[...]

    def step(k, carry):
        c, ratios = carry
        e_row = (lane == k).astype(jnp.float32)
        e_col = (sub == k).astype(jnp.float32)
        row_row = m_ref[pl.ds(k, 1), :]
        col_row = mt_ref[pl.ds(k, 1), :]
        row_col = jnp.sum(mt * e_row, axis=1, keepdims=True)
        left = jnp.sum(c * row_col, axis=0, keepdims=True)
        right = jnp.sum(c * col_row, axis=1, keepdims=True)
        diag = jnp.sum(row_row * e_row, axis=1, keepdims=True)
        lc = jnp.sum(left * col_row, axis=1, keepdims=True)
        ratio = 1.0 + diag - lc
        flag = jnp.sum(acc * e_row, axis=1, keepdims=True)
        c = c + flag * ((right - e_col) * (left - e_row)) / ratio
        ratios = ratios + e_row * ratio
        return c, ratios

    c0 = jnp.zeros((n, n), jnp.float32)
    r0 = jnp.zeros((1, n), jnp.float32)
    c, ratios = lax.fori_loop(0, n, step, (c0, r0))
    c_ref[...] = c
    r_ref[...] = ratios


def border(intersection, accepted):
    n = intersection.shape[0]
    vm = pl.BlockSpec(memory_space=pltpu.VMEM)
    c, r = pl.pallas_call(
        _border_kernel,
        out_shape=(jax.ShapeDtypeStruct((n, n), jnp.float32), jax.ShapeDtypeStruct((1, n), jnp.float32)),
        in_specs=[vm, vm, vm],
        out_specs=(vm, vm),
    )(intersection, intersection.T, accepted.astype(jnp.float32).reshape(1, n))
    return c, r.reshape(n)


def ring_rs(x, axis, n, d):
    i = lax.axis_index(axis)
    B = x.shape[1] // n
    chunk = lambda c: lax.dynamic_slice_in_dim(x, c * B, B, 1)
    perm = [(j, (j + d) % n) for j in range(n)]
    acc = chunk((i - d) % n)
    for s in range(1, n):
        acc = lax.ppermute(acc, axis, perm)
        acc = acc + chunk((i - d * (s + 1)) % n)
    return acc

def ring_ag(x, axis, n, d):
    i = lax.axis_index(axis)
    B = x.shape[1]
    out = jnp.zeros(x.shape[:1] + (n * B,), x.dtype)
    out = lax.dynamic_update_slice_in_dim(out, x, i * B, 1)
    perm = [(j, (j + d) % n) for j in range(n)]
    cur = x
    for s in range(1, n):
        cur = lax.ppermute(cur, axis, perm)
        out = lax.dynamic_update_slice_in_dim(out, cur, ((i - d * s) % n) * B, 1)
    return out

def rs(x, axis, n, bidir):
    if not bidir:
        return ring_rs(x, axis, n, 1)
    h = x.shape[0] // 2
    return jnp.concatenate([ring_rs(x[:h], axis, n, 1), ring_rs(x[h:], axis, n, -1)], axis=0)

def ag(x, axis, n, bidir):
    if not bidir:
        return ring_ag(x, axis, n, 1)
    h = x.shape[0] // 2
    return jnp.concatenate([ring_ag(x[:h], axis, n, 1), ring_ag(x[h:], axis, n, -1)], axis=0)

def ring_allreduce(x, phases):
    for axis, n, b in phases:
        x = rs(x, axis, n, b)
    for axis, n, b in reversed(phases):
        x = ag(x, axis, n, b)
    return x


def on_device(inverse_rows, row_values, orbital_blocks, moved, accepted):
    row_count = inverse_rows.shape[0]
    block_width = row_values.shape[2]
    blocks_here = row_count // block_width
    owned_blocks = lax.axis_index(ELEC) * blocks_here + jnp.arange(blocks_here, dtype=jnp.int32)
    onehot = (orbital_blocks[:, :, None] == owned_blocks[None, None, :]).astype(jnp.float32)
    change = jnp.einsum("ksb,kst->kbt", onehot, row_values, precision=HI).reshape(MOVES, row_count)
    picked = jnp.take(inverse_rows, moved, axis=1)
    local_weights = jnp.dot(change, inverse_rows, precision=HI)
    full_weights = ring_allreduce(local_weights, PHASES)
    intersection = jnp.take(full_weights, moved, axis=1)
    coupling, ratios = border(intersection, accepted)
    factor = jnp.dot(picked, coupling, precision=HI)
    new_inverse = inverse_rows - jnp.dot(factor, full_weights, precision=HI)
    return (new_inverse, ratios)


ELEC = ("x", "z", "y")
PHASES = (("z", 8, True), ("y", 4, False), ("x", 4, False))


def solution(mesh):
    walkers, elec = mesh.devices.shape
    torus = mesh.devices.reshape(walkers, 4, 8, elec // 32)
    mesh = Mesh(torus, ("walker",) + ELEC)
    rows = ("walker",) + ELEC
    placed = (
        P(rows, None),
        P("walker", None, None),
        P("walker", None),
        P("walker"),
        P("walker"),
    )
    return jax.shard_map(
        on_device,
        mesh=mesh,
        in_specs=placed,
        out_specs=(P(rows, None), P("walker")),
        check_vma=False,
    )
```

```python
import jax
import jax.numpy as jnp
from jax import lax
from jax.sharding import Mesh, PartitionSpec as P
from jax.experimental import pallas as pl
from jax.experimental.pallas import tpu as pltpu

MOVES = 64


HI = lax.Precision.HIGHEST


def border_step(coupling, row_vec, col_vec, accept_flag, unit_row):
    left_vec = jnp.dot(row_vec, coupling, precision=HI)
    right_vec = jnp.dot(coupling, col_vec, precision=HI)
    det_ratio = (
        1.0 + jnp.dot(row_vec, unit_row, precision=HI) - jnp.dot(left_vec, col_vec, precision=HI)
    )
    coupling = (
        coupling + accept_flag * jnp.outer(right_vec - unit_row, left_vec - unit_row) / det_ratio
    )
    return (coupling, det_ratio)


def run_border(intersection, accepted):

    def one_step(coupling, step_items):
        row_vec, col_vec, accept_flag, unit_row = step_items
        return border_step(coupling, row_vec, col_vec, accept_flag, unit_row)

    start_value = jnp.zeros((MOVES, MOVES), jnp.float32)
    step_items = (
        intersection,
        intersection.T,
        accepted.astype(jnp.float32),
        jnp.eye(MOVES, dtype=jnp.float32),
    )
    return lax.scan(one_step, start_value, step_items)


def _border_kernel(m_ref, mt_ref, acc_ref, c_ref, r_ref):
    n = m_ref.shape[0]
    lane = lax.broadcasted_iota(jnp.int32, (1, n), 1)
    sub = lax.broadcasted_iota(jnp.int32, (n, 1), 0)
    mt = mt_ref[...]
    acc = acc_ref[...]

    def step(k, carry):
        c, ratios = carry
        e_row = (lane == k).astype(jnp.float32)
        e_col = (sub == k).astype(jnp.float32)
        row_row = m_ref[pl.ds(k, 1), :]
        col_row = mt_ref[pl.ds(k, 1), :]
        row_col = jnp.sum(mt * e_row, axis=1, keepdims=True)
        left = jnp.sum(c * row_col, axis=0, keepdims=True)
        right = jnp.sum(c * col_row, axis=1, keepdims=True)
        diag = jnp.sum(row_row * e_row, axis=1, keepdims=True)
        lc = jnp.sum(left * col_row, axis=1, keepdims=True)
        ratio = 1.0 + diag - lc
        flag = jnp.sum(acc * e_row, axis=1, keepdims=True)
        c = c + flag * ((right - e_col) * (left - e_row)) / ratio
        ratios = ratios + e_row * ratio
        return c, ratios

    c0 = jnp.zeros((n, n), jnp.float32)
    r0 = jnp.zeros((1, n), jnp.float32)
    c, ratios = lax.fori_loop(0, n, step, (c0, r0))
    c_ref[...] = c
    r_ref[...] = ratios


def border(intersection, accepted):
    n = intersection.shape[0]
    vm = pl.BlockSpec(memory_space=pltpu.VMEM)
    c, r = pl.pallas_call(
        _border_kernel,
        out_shape=(jax.ShapeDtypeStruct((n, n), jnp.float32), jax.ShapeDtypeStruct((1, n), jnp.float32)),
        in_specs=[vm, vm, vm],
        out_specs=(vm, vm),
    )(intersection, intersection.T, accepted.astype(jnp.float32).reshape(1, n))
    return c, r.reshape(n)


def shift_perm(n, d):
    return [(j, (j + d) % n) for j in range(n)]


def half_ring_rs(x, axis, n):
    if n == 1:
        return x
    i = lax.axis_index(axis)
    width = x.shape[1] // n
    chunk = lambda c: lax.dynamic_slice_in_dim(x, (c % n) * width, width, 1)
    up, down = n // 2, n - 1 - n // 2
    cw, ccw = chunk(i + up), chunk(i - down)
    for s in range(1, up + 1):
        cw = lax.ppermute(cw, axis, shift_perm(n, 1))
        if s <= down:
            ccw = lax.ppermute(ccw, axis, shift_perm(n, -1))
        if s < up:
            cw = cw + chunk(i + up - s)
        if s < down:
            ccw = ccw + chunk(i - down + s)
    if down == 0:
        return chunk(i) + cw
    return chunk(i) + cw + ccw


def half_ring_ag(x, axis, n):
    if n == 1:
        return x
    i = lax.axis_index(axis)
    width = x.shape[1]
    up, down = n // 2, n - 1 - n // 2
    out = jnp.zeros(x.shape[:1] + (n * width,), x.dtype)
    out = lax.dynamic_update_slice_in_dim(out, x, i * width, 1)
    cw, ccw = x, x
    for s in range(1, up + 1):
        cw = lax.ppermute(cw, axis, shift_perm(n, 1))
        out = lax.dynamic_update_slice_in_dim(out, cw, ((i - s) % n) * width, 1)
        if s <= down:
            ccw = lax.ppermute(ccw, axis, shift_perm(n, -1))
            out = lax.dynamic_update_slice_in_dim(out, ccw, ((i + s) % n) * width, 1)
    return out


def ring_allreduce(x, phases):
    for axis, n in phases:
        x = half_ring_rs(x, axis, n)
    for axis, n in reversed(phases):
        x = half_ring_ag(x, axis, n)
    return x


def on_device(inverse_rows, row_values, orbital_blocks, moved, accepted):
    row_count = inverse_rows.shape[0]
    block_width = row_values.shape[2]
    blocks_here = row_count // block_width
    owned_blocks = lax.axis_index(ELEC) * blocks_here + jnp.arange(blocks_here, dtype=jnp.int32)
    onehot = (orbital_blocks[:, :, None] == owned_blocks[None, None, :]).astype(jnp.float32)
    change = jnp.einsum("ksb,kst->kbt", onehot, row_values, precision=HI).reshape(MOVES, row_count)
    picked = jnp.take(inverse_rows, moved, axis=1)
    local_weights = jnp.dot(change, inverse_rows, precision=HI)
    full_weights = ring_allreduce(local_weights, PHASES)
    intersection = jnp.take(full_weights, moved, axis=1)
    coupling, ratios = border(intersection, accepted)
    factor = jnp.dot(picked, coupling, precision=HI)
    new_inverse = inverse_rows - jnp.dot(factor, full_weights, precision=HI)
    return (new_inverse, ratios)


ELEC = ("x", "z", "y")
PHASES = (("z", 8), ("y", 4), ("x", 4))


def solution(mesh):
    walkers, elec = mesh.devices.shape
    torus = mesh.devices.reshape(walkers, 4, 8, elec // 32)
    mesh = Mesh(torus, ("walker",) + ELEC)
    rows = ("walker",) + ELEC
    placed = (
        P(rows, None),
        P("walker", None, None),
        P("walker", None),
        P("walker"),
        P("walker"),
    )
    return jax.shard_map(
        on_device,
        mesh=mesh,
        in_specs=placed,
        out_specs=(P(rows, None), P("walker")),
        check_vma=False,
    )
```

```python
import jax
import jax.numpy as jnp
from jax import lax
from jax.sharding import Mesh, PartitionSpec as P
from jax.experimental import pallas as pl
from jax.experimental.pallas import tpu as pltpu

MOVES = 64


HI = lax.Precision.HIGHEST


def border_step(coupling, row_vec, col_vec, accept_flag, unit_row):
    left_vec = jnp.dot(row_vec, coupling, precision=HI)
    right_vec = jnp.dot(coupling, col_vec, precision=HI)
    det_ratio = (
        1.0 + jnp.dot(row_vec, unit_row, precision=HI) - jnp.dot(left_vec, col_vec, precision=HI)
    )
    coupling = (
        coupling + accept_flag * jnp.outer(right_vec - unit_row, left_vec - unit_row) / det_ratio
    )
    return (coupling, det_ratio)


def run_border(intersection, accepted):

    def one_step(coupling, step_items):
        row_vec, col_vec, accept_flag, unit_row = step_items
        return border_step(coupling, row_vec, col_vec, accept_flag, unit_row)

    start_value = jnp.zeros((MOVES, MOVES), jnp.float32)
    step_items = (
        intersection,
        intersection.T,
        accepted.astype(jnp.float32),
        jnp.eye(MOVES, dtype=jnp.float32),
    )
    return lax.scan(one_step, start_value, step_items)


def _border_kernel(m_ref, mt_ref, acc_ref, c_ref, r_ref):
    n = m_ref.shape[0]
    lane = lax.broadcasted_iota(jnp.int32, (1, n), 1)
    sub = lax.broadcasted_iota(jnp.int32, (n, 1), 0)
    mt = mt_ref[...]
    acc = acc_ref[...]

    def step(k, carry):
        c, ratios = carry
        e_row = (lane == k).astype(jnp.float32)
        e_col = (sub == k).astype(jnp.float32)
        row_row = m_ref[pl.ds(k, 1), :]
        col_row = mt_ref[pl.ds(k, 1), :]
        row_col = jnp.sum(mt * e_row, axis=1, keepdims=True)
        left = jnp.sum(c * row_col, axis=0, keepdims=True)
        right = jnp.sum(c * col_row, axis=1, keepdims=True)
        diag = jnp.sum(row_row * e_row, axis=1, keepdims=True)
        lc = jnp.sum(left * col_row, axis=1, keepdims=True)
        ratio = 1.0 + diag - lc
        flag = jnp.sum(acc * e_row, axis=1, keepdims=True)
        c = c + flag * ((right - e_col) * (left - e_row)) / ratio
        ratios = ratios + e_row * ratio
        return c, ratios

    c0 = jnp.zeros((n, n), jnp.float32)
    r0 = jnp.zeros((1, n), jnp.float32)
    c, ratios = lax.fori_loop(0, n, step, (c0, r0), unroll=8)
    c_ref[...] = c
    r_ref[...] = ratios


def border(intersection, accepted):
    n = intersection.shape[0]
    vm = pl.BlockSpec(memory_space=pltpu.VMEM)
    c, r = pl.pallas_call(
        _border_kernel,
        out_shape=(jax.ShapeDtypeStruct((n, n), jnp.float32), jax.ShapeDtypeStruct((1, n), jnp.float32)),
        in_specs=[vm, vm, vm],
        out_specs=(vm, vm),
    )(intersection, intersection.T, accepted.astype(jnp.float32).reshape(1, n))
    return c, r.reshape(n)


def shift_perm(n, d):
    return [(j, (j + d) % n) for j in range(n)]


def half_ring_rs(x, axis, n):
    if n == 1:
        return x
    i = lax.axis_index(axis)
    width = x.shape[1] // n
    chunk = lambda c: lax.dynamic_slice_in_dim(x, (c % n) * width, width, 1)
    up, down = n // 2, n - 1 - n // 2
    cw, ccw = chunk(i + up), chunk(i - down)
    for s in range(1, up + 1):
        cw = lax.ppermute(cw, axis, shift_perm(n, 1))
        if s <= down:
            ccw = lax.ppermute(ccw, axis, shift_perm(n, -1))
        if s < up:
            cw = cw + chunk(i + up - s)
        if s < down:
            ccw = ccw + chunk(i - down + s)
    if down == 0:
        return chunk(i) + cw
    return chunk(i) + cw + ccw


def half_ring_ag(x, axis, n):
    if n == 1:
        return x
    i = lax.axis_index(axis)
    width = x.shape[1]
    up, down = n // 2, n - 1 - n // 2
    out = jnp.zeros(x.shape[:1] + (n * width,), x.dtype)
    out = lax.dynamic_update_slice_in_dim(out, x, i * width, 1)
    cw, ccw = x, x
    for s in range(1, up + 1):
        cw = lax.ppermute(cw, axis, shift_perm(n, 1))
        out = lax.dynamic_update_slice_in_dim(out, cw, ((i - s) % n) * width, 1)
        if s <= down:
            ccw = lax.ppermute(ccw, axis, shift_perm(n, -1))
            out = lax.dynamic_update_slice_in_dim(out, ccw, ((i + s) % n) * width, 1)
    return out

def direct_rs(x, axis, n):
    i = lax.axis_index(axis)
    width = x.shape[1] // n
    chunk = lambda c: lax.dynamic_slice_in_dim(x, (c % n) * width, width, 1)
    total = chunk(i)
    for d in SHIFTS[n]:
        total = total + lax.ppermute(chunk(i + d), axis, shift_perm(n, d))
    return total


def direct_ag(x, axis, n):
    i = lax.axis_index(axis)
    width = x.shape[1]
    out = jnp.zeros(x.shape[:1] + (n * width,), x.dtype)
    out = lax.dynamic_update_slice_in_dim(out, x, i * width, 1)
    for d in SHIFTS[n]:
        got = lax.ppermute(x, axis, shift_perm(n, d))
        out = lax.dynamic_update_slice_in_dim(out, got, ((i - d) % n) * width, 1)
    return out


SHIFTS = {2: (1,), 4: (1, -1, 2)}


def ring_allreduce(x, phases):
    for axis, n in phases:
        x = direct_rs(x, axis, n) if n in SHIFTS else half_ring_rs(x, axis, n)
    for axis, n in reversed(phases):
        x = direct_ag(x, axis, n) if n in SHIFTS else half_ring_ag(x, axis, n)
    return x


def on_device(inverse_rows, row_values, orbital_blocks, moved, accepted):
    row_count = inverse_rows.shape[0]
    block_width = row_values.shape[2]
    blocks_here = row_count // block_width
    owned_blocks = lax.axis_index(ELEC) * blocks_here + jnp.arange(blocks_here, dtype=jnp.int32)
    onehot = (orbital_blocks[:, :, None] == owned_blocks[None, None, :]).astype(jnp.float32)
    change = jnp.einsum("ksb,kst->kbt", onehot, row_values, precision=HI).reshape(MOVES, row_count)
    picked = jnp.take(inverse_rows, moved, axis=1)
    local_weights = jnp.dot(change, inverse_rows, precision=HI)
    full_weights = ring_allreduce(local_weights, PHASES)
    intersection = jnp.take(full_weights, moved, axis=1)
    coupling, ratios = border(intersection, accepted)
    factor = jnp.dot(picked, coupling, precision=HI)
    new_inverse = inverse_rows - jnp.dot(factor, full_weights, precision=HI)
    return (new_inverse, ratios)


ELEC = ("x", "z", "y")
PHASES = (("z", 8), ("y", 4), ("x", 4))


def solution(mesh):
    walkers, elec = mesh.devices.shape
    torus = mesh.devices.reshape(walkers, 4, 8, elec // 32)
    mesh = Mesh(torus, ("walker",) + ELEC)
    rows = ("walker",) + ELEC
    placed = (
        P(rows, None),
        P("walker", None, None),
        P("walker", None),
        P("walker"),
        P("walker"),
    )
    return jax.shard_map(
        on_device,
        mesh=mesh,
        in_specs=placed,
        out_specs=(P(rows, None), P("walker")),
        check_vma=False,
    )
```

```python
import jax
import jax.numpy as jnp
from jax import lax
from jax.sharding import Mesh, PartitionSpec as P
from jax.experimental import pallas as pl
from jax.experimental.pallas import tpu as pltpu

MOVES = 64


HI = lax.Precision.HIGHEST


def border_step(coupling, row_vec, col_vec, accept_flag, unit_row):
    left_vec = jnp.dot(row_vec, coupling, precision=HI)
    right_vec = jnp.dot(coupling, col_vec, precision=HI)
    det_ratio = (
        1.0 + jnp.dot(row_vec, unit_row, precision=HI) - jnp.dot(left_vec, col_vec, precision=HI)
    )
    coupling = (
        coupling + accept_flag * jnp.outer(right_vec - unit_row, left_vec - unit_row) / det_ratio
    )
    return (coupling, det_ratio)


def run_border(intersection, accepted):

    def one_step(coupling, step_items):
        row_vec, col_vec, accept_flag, unit_row = step_items
        return border_step(coupling, row_vec, col_vec, accept_flag, unit_row)

    start_value = jnp.zeros((MOVES, MOVES), jnp.float32)
    step_items = (
        intersection,
        intersection.T,
        accepted.astype(jnp.float32),
        jnp.eye(MOVES, dtype=jnp.float32),
    )
    return lax.scan(one_step, start_value, step_items)


def _border_kernel(m_ref, mt_ref, acc_ref, c_ref, r_ref):
    n = m_ref.shape[0]
    lane = lax.broadcasted_iota(jnp.int32, (1, n), 1)
    sub = lax.broadcasted_iota(jnp.int32, (n, 1), 0)
    mt = mt_ref[...]
    acc = acc_ref[...]

    def step(k, carry):
        c, ratios = carry
        e_row = (lane == k).astype(jnp.float32)
        e_col = (sub == k).astype(jnp.float32)
        row_row = m_ref[pl.ds(k, 1), :]
        col_row = mt_ref[pl.ds(k, 1), :]
        row_col = jnp.sum(mt * e_row, axis=1, keepdims=True)
        left = jnp.sum(c * row_col, axis=0, keepdims=True)
        right = jnp.sum(c * col_row, axis=1, keepdims=True)
        diag = jnp.sum(row_row * e_row, axis=1, keepdims=True)
        lc = jnp.sum(left * col_row, axis=1, keepdims=True)
        ratio = 1.0 + diag - lc
        flag = jnp.sum(acc * e_row, axis=1, keepdims=True)
        c = c + flag * ((right - e_col) * (left - e_row)) / ratio
        ratios = ratios + e_row * ratio
        return c, ratios

    c0 = jnp.zeros((n, n), jnp.float32)
    r0 = jnp.zeros((1, n), jnp.float32)
    c, ratios = lax.fori_loop(0, n, step, (c0, r0), unroll=8)
    c_ref[...] = c
    r_ref[...] = ratios


def border(intersection, accepted):
    n = intersection.shape[0]
    vm = pl.BlockSpec(memory_space=pltpu.VMEM)
    c, r = pl.pallas_call(
        _border_kernel,
        out_shape=(jax.ShapeDtypeStruct((n, n), jnp.float32), jax.ShapeDtypeStruct((1, n), jnp.float32)),
        in_specs=[vm, vm, vm],
        out_specs=(vm, vm),
    )(intersection, intersection.T, accepted.astype(jnp.float32).reshape(1, n))
    return c, r.reshape(n)


def shift_perm(n, d):
    return [(j, (j + d) % n) for j in range(n)]


def half_ring_rs(x, axis, n):
    if n == 1:
        return x
    i = lax.axis_index(axis)
    width = x.shape[1] // n
    chunk = lambda c: lax.dynamic_slice_in_dim(x, (c % n) * width, width, 1)
    up, down = n // 2, n - 1 - n // 2
    cw, ccw = chunk(i + up), chunk(i - down)
    for s in range(1, up + 1):
        cw = lax.ppermute(cw, axis, shift_perm(n, 1))
        if s <= down:
            ccw = lax.ppermute(ccw, axis, shift_perm(n, -1))
        if s < up:
            cw = cw + chunk(i + up - s)
        if s < down:
            ccw = ccw + chunk(i - down + s)
    if down == 0:
        return chunk(i) + cw
    return chunk(i) + cw + ccw


def half_ring_ag(x, axis, n):
    if n == 1:
        return x
    i = lax.axis_index(axis)
    width = x.shape[1]
    up, down = n // 2, n - 1 - n // 2
    out = jnp.zeros(x.shape[:1] + (n * width,), x.dtype)
    out = lax.dynamic_update_slice_in_dim(out, x, i * width, 1)
    cw, ccw = x, x
    for s in range(1, up + 1):
        cw = lax.ppermute(cw, axis, shift_perm(n, 1))
        out = lax.dynamic_update_slice_in_dim(out, cw, ((i - s) % n) * width, 1)
        if s <= down:
            ccw = lax.ppermute(ccw, axis, shift_perm(n, -1))
            out = lax.dynamic_update_slice_in_dim(out, ccw, ((i + s) % n) * width, 1)
    return out

def direct_rs(x, axis, n):
    i = lax.axis_index(axis)
    width = x.shape[1] // n
    chunk = lambda c: lax.dynamic_slice_in_dim(x, (c % n) * width, width, 1)
    total = chunk(i)
    for d in SHIFTS[n]:
        total = total + lax.ppermute(chunk(i + d), axis, shift_perm(n, d))
    return total


def direct_ag(x, axis, n):
    i = lax.axis_index(axis)
    width = x.shape[1]
    out = jnp.zeros(x.shape[:1] + (n * width,), x.dtype)
    out = lax.dynamic_update_slice_in_dim(out, x, i * width, 1)
    for d in SHIFTS[n]:
        got = lax.ppermute(x, axis, shift_perm(n, d))
        out = lax.dynamic_update_slice_in_dim(out, got, ((i - d) % n) * width, 1)
    return out


SHIFTS = {2: (1,), 4: (1, -1, 2)}


def ring_allreduce(x, phases):
    for axis, n in phases:
        x = direct_rs(x, axis, n) if n in SHIFTS else half_ring_rs(x, axis, n)
    for axis, n in reversed(phases):
        x = direct_ag(x, axis, n) if n in SHIFTS else half_ring_ag(x, axis, n)
    return x


def on_device(inverse_rows, row_values, orbital_blocks, moved, accepted):
    row_count = inverse_rows.shape[0]
    block_width = row_values.shape[2]
    blocks_here = row_count // block_width
    owned_blocks = lax.axis_index(ELEC) * blocks_here + jnp.arange(blocks_here, dtype=jnp.int32)
    onehot = (orbital_blocks[:, :, None] == owned_blocks[None, None, :]).astype(jnp.float32)
    change = jnp.einsum("ksb,kst->kbt", onehot, row_values, precision=HI).reshape(MOVES, row_count)
    picked = jnp.take(inverse_rows, moved, axis=1)
    local_weights = jnp.dot(change, inverse_rows, precision=HI)
    full_weights = ring_allreduce(local_weights, PHASES)
    electrons = full_weights.shape[1]
    pick = (lax.broadcasted_iota(jnp.int32, (electrons, MOVES), 0) == moved[None, :]).astype(jnp.float32)
    intersection = jnp.dot(full_weights, pick, precision=HI)
    coupling, ratios = border(intersection, accepted)
    factor = jnp.dot(picked, coupling, precision=HI)
    new_inverse = inverse_rows - jnp.dot(factor, full_weights, precision=HI)
    return (new_inverse, ratios)


ELEC = ("x", "z", "y")
PHASES = (("z", 8), ("y", 4), ("x", 4))


def solution(mesh):
    walkers, elec = mesh.devices.shape
    torus = mesh.devices.reshape(walkers, 4, 8, elec // 32)
    mesh = Mesh(torus, ("walker",) + ELEC)
    rows = ("walker",) + ELEC
    placed = (
        P(rows, None),
        P("walker", None, None),
        P("walker", None),
        P("walker"),
        P("walker"),
    )
    return jax.shard_map(
        on_device,
        mesh=mesh,
        in_specs=placed,
        out_specs=(P(rows, None), P("walker")),
        check_vma=False,
    )
```

```python
import jax
import jax.numpy as jnp
from jax import lax
from jax.sharding import Mesh, PartitionSpec as P
from jax.experimental import pallas as pl
from jax.experimental.pallas import tpu as pltpu

MOVES = 64


HI = lax.Precision.HIGHEST


def border_step(coupling, row_vec, col_vec, accept_flag, unit_row):
    left_vec = jnp.dot(row_vec, coupling, precision=HI)
    right_vec = jnp.dot(coupling, col_vec, precision=HI)
    det_ratio = (
        1.0 + jnp.dot(row_vec, unit_row, precision=HI) - jnp.dot(left_vec, col_vec, precision=HI)
    )
    coupling = (
        coupling + accept_flag * jnp.outer(right_vec - unit_row, left_vec - unit_row) / det_ratio
    )
    return (coupling, det_ratio)


def run_border(intersection, accepted):

    def one_step(coupling, step_items):
        row_vec, col_vec, accept_flag, unit_row = step_items
        return border_step(coupling, row_vec, col_vec, accept_flag, unit_row)

    start_value = jnp.zeros((MOVES, MOVES), jnp.float32)
    step_items = (
        intersection,
        intersection.T,
        accepted.astype(jnp.float32),
        jnp.eye(MOVES, dtype=jnp.float32),
    )
    return lax.scan(one_step, start_value, step_items)


def _border_kernel(m_ref, mt_ref, acc_ref, c_ref, r_ref):
    n = m_ref.shape[0]
    lane = lax.broadcasted_iota(jnp.int32, (1, n), 1)
    sub = lax.broadcasted_iota(jnp.int32, (n, 1), 0)
    mt = mt_ref[...]
    acc = acc_ref[...]

    def step(k, carry):
        c, ratios = carry
        e_row = (lane == k).astype(jnp.float32)
        e_col = (sub == k).astype(jnp.float32)
        row_row = m_ref[pl.ds(k, 1), :]
        col_row = mt_ref[pl.ds(k, 1), :]
        row_col = jnp.sum(mt * e_row, axis=1, keepdims=True)
        left = jnp.sum(c * row_col, axis=0, keepdims=True)
        right = jnp.sum(c * col_row, axis=1, keepdims=True)
        diag = jnp.sum(row_row * e_row, axis=1, keepdims=True)
        lc = jnp.sum(left * col_row, axis=1, keepdims=True)
        ratio = 1.0 + diag - lc
        flag = jnp.sum(acc * e_row, axis=1, keepdims=True)
        c = c + flag * ((right - e_col) * (left - e_row)) / ratio
        ratios = ratios + e_row * ratio
        return c, ratios

    c0 = jnp.zeros((n, n), jnp.float32)
    r0 = jnp.zeros((1, n), jnp.float32)
    c, ratios = lax.fori_loop(0, n, step, (c0, r0), unroll=8)
    c_ref[...] = c
    r_ref[...] = ratios


def border(intersection, accepted):
    n = intersection.shape[0]
    vm = pl.BlockSpec(memory_space=pltpu.VMEM)
    c, r = pl.pallas_call(
        _border_kernel,
        out_shape=(jax.ShapeDtypeStruct((n, n), jnp.float32), jax.ShapeDtypeStruct((1, n), jnp.float32)),
        in_specs=[vm, vm, vm],
        out_specs=(vm, vm),
    )(intersection, intersection.T, accepted.astype(jnp.float32).reshape(1, n))
    return c, r.reshape(n)


def shift_perm(n, d):
    return [(j, (j + d) % n) for j in range(n)]


def half_ring_rs(x, axis, n):
    if n == 1:
        return x
    i = lax.axis_index(axis)
    width = x.shape[1] // n
    chunk = lambda c: lax.dynamic_slice_in_dim(x, (c % n) * width, width, 1)
    up, down = n // 2, n - 1 - n // 2
    cw, ccw = chunk(i + up), chunk(i - down)
    for s in range(1, up + 1):
        cw = lax.ppermute(cw, axis, shift_perm(n, 1))
        if s <= down:
            ccw = lax.ppermute(ccw, axis, shift_perm(n, -1))
        if s < up:
            cw = cw + chunk(i + up - s)
        if s < down:
            ccw = ccw + chunk(i - down + s)
    if down == 0:
        return chunk(i) + cw
    return chunk(i) + cw + ccw


def half_ring_ag(x, axis, n):
    if n == 1:
        return x
    i = lax.axis_index(axis)
    width = x.shape[1]
    up, down = n // 2, n - 1 - n // 2
    out = jnp.zeros(x.shape[:1] + (n * width,), x.dtype)
    out = lax.dynamic_update_slice_in_dim(out, x, i * width, 1)
    cw, ccw = x, x
    for s in range(1, up + 1):
        cw = lax.ppermute(cw, axis, shift_perm(n, 1))
        out = lax.dynamic_update_slice_in_dim(out, cw, ((i - s) % n) * width, 1)
        if s <= down:
            ccw = lax.ppermute(ccw, axis, shift_perm(n, -1))
            out = lax.dynamic_update_slice_in_dim(out, ccw, ((i + s) % n) * width, 1)
    return out

def direct_rs(x, axis, n):
    i = lax.axis_index(axis)
    width = x.shape[1] // n
    chunk = lambda c: lax.dynamic_slice_in_dim(x, (c % n) * width, width, 1)
    total = chunk(i)
    for d in SHIFTS[n]:
        total = total + lax.ppermute(chunk(i + d), axis, shift_perm(n, d))
    return total


def direct_ag(x, axis, n):
    i = lax.axis_index(axis)
    width = x.shape[1]
    out = jnp.zeros(x.shape[:1] + (n * width,), x.dtype)
    out = lax.dynamic_update_slice_in_dim(out, x, i * width, 1)
    for d in SHIFTS[n]:
        got = lax.ppermute(x, axis, shift_perm(n, d))
        out = lax.dynamic_update_slice_in_dim(out, got, ((i - d) % n) * width, 1)
    return out


SHIFTS = {2: (1,), 4: (1, -1, 2)}


def ring_allreduce(x, phases):
    for axis, n in phases:
        x = direct_rs(x, axis, n) if n in SHIFTS else half_ring_rs(x, axis, n)
    for axis, n in reversed(phases):
        x = direct_ag(x, axis, n) if n in SHIFTS else half_ring_ag(x, axis, n)
    return x


def butterfly_allreduce(x, axes):
    for axis, n in axes:
        bit = 1
        while bit < n:
            x = x + lax.ppermute(x, axis, [(j, j ^ bit) for j in range(n)])
            bit *= 2
    return x


def on_device(inverse_rows, row_values, orbital_blocks, moved, accepted):
    row_count = inverse_rows.shape[0]
    block_width = row_values.shape[2]
    blocks_here = row_count // block_width
    owned_blocks = lax.axis_index(ELEC) * blocks_here + jnp.arange(blocks_here, dtype=jnp.int32)
    onehot = (orbital_blocks[:, :, None] == owned_blocks[None, None, :]).astype(jnp.float32)
    change = jnp.einsum("ksb,kst->kbt", onehot, row_values, precision=HI).reshape(MOVES, row_count)
    picked = jnp.take(inverse_rows, moved, axis=1)
    local_weights = jnp.dot(change, inverse_rows, precision=HI)
    full_weights = ring_allreduce(local_weights, PHASES)
    intersection = butterfly_allreduce(jnp.dot(change, picked, precision=HI), PHASES)
    coupling, ratios = border(intersection, accepted)
    factor = jnp.dot(picked, coupling, precision=HI)
    new_inverse = inverse_rows - jnp.dot(factor, full_weights, precision=HI)
    return (new_inverse, ratios)


ELEC = ("x", "z", "y")
PHASES = (("z", 8), ("y", 4), ("x", 4))


def solution(mesh):
    walkers, elec = mesh.devices.shape
    torus = mesh.devices.reshape(walkers, 4, 8, elec // 32)
    mesh = Mesh(torus, ("walker",) + ELEC)
    rows = ("walker",) + ELEC
    placed = (
        P(rows, None),
        P("walker", None, None),
        P("walker", None),
        P("walker"),
        P("walker"),
    )
    return jax.shard_map(
        on_device,
        mesh=mesh,
        in_specs=placed,
        out_specs=(P(rows, None), P("walker")),
        check_vma=False,
    )
```

```python
import jax
import jax.numpy as jnp
from jax import lax
from jax.sharding import Mesh, PartitionSpec as P
from jax.experimental import pallas as pl
from jax.experimental.pallas import tpu as pltpu

MOVES = 64


HI = lax.Precision.HIGHEST


def border_step(coupling, row_vec, col_vec, accept_flag, unit_row):
    left_vec = jnp.dot(row_vec, coupling, precision=HI)
    right_vec = jnp.dot(coupling, col_vec, precision=HI)
    det_ratio = (
        1.0 + jnp.dot(row_vec, unit_row, precision=HI) - jnp.dot(left_vec, col_vec, precision=HI)
    )
    coupling = (
        coupling + accept_flag * jnp.outer(right_vec - unit_row, left_vec - unit_row) / det_ratio
    )
    return (coupling, det_ratio)


def run_border(intersection, accepted):

    def one_step(coupling, step_items):
        row_vec, col_vec, accept_flag, unit_row = step_items
        return border_step(coupling, row_vec, col_vec, accept_flag, unit_row)

    start_value = jnp.zeros((MOVES, MOVES), jnp.float32)
    step_items = (
        intersection,
        intersection.T,
        accepted.astype(jnp.float32),
        jnp.eye(MOVES, dtype=jnp.float32),
    )
    return lax.scan(one_step, start_value, step_items)


def _border_kernel(m_ref, mt_ref, acc_ref, c_ref, r_ref):
    n = m_ref.shape[0]
    lane = lax.broadcasted_iota(jnp.int32, (1, n), 1)
    sub = lax.broadcasted_iota(jnp.int32, (n, 1), 0)
    mt = mt_ref[...]
    acc = acc_ref[...]

    def step(k, carry):
        c, ratios = carry
        e_row = (lane == k).astype(jnp.float32)
        e_col = (sub == k).astype(jnp.float32)
        row_row = m_ref[pl.ds(k, 1), :]
        col_row = mt_ref[pl.ds(k, 1), :]
        row_col = jnp.sum(mt * e_row, axis=1, keepdims=True)
        left = jnp.sum(c * row_col, axis=0, keepdims=True)
        right = jnp.sum(c * col_row, axis=1, keepdims=True)
        diag = jnp.sum(row_row * e_row, axis=1, keepdims=True)
        lc = jnp.sum(left * col_row, axis=1, keepdims=True)
        ratio = 1.0 + diag - lc
        flag = jnp.sum(acc * e_row, axis=1, keepdims=True)
        c = c + flag * ((right - e_col) * (left - e_row)) / ratio
        ratios = ratios + e_row * ratio
        return c, ratios

    c0 = jnp.zeros((n, n), jnp.float32)
    r0 = jnp.zeros((1, n), jnp.float32)
    c, ratios = lax.fori_loop(0, n, step, (c0, r0), unroll=8)
    c_ref[...] = c
    r_ref[...] = ratios


def border(intersection, accepted):
    n = intersection.shape[0]
    vm = pl.BlockSpec(memory_space=pltpu.VMEM)
    c, r = pl.pallas_call(
        _border_kernel,
        out_shape=(jax.ShapeDtypeStruct((n, n), jnp.float32), jax.ShapeDtypeStruct((1, n), jnp.float32)),
        in_specs=[vm, vm, vm],
        out_specs=(vm, vm),
    )(intersection, intersection.T, accepted.astype(jnp.float32).reshape(1, n))
    return c, r.reshape(n)


def shift_perm(n, d):
    return [(j, (j + d) % n) for j in range(n)]


def mirrored(axis, n):
    walker = lax.axis_index("walker")
    i = lax.axis_index(axis)
    virtual = (i + walker * (n - 2 * i)) % n
    ahead = [(j, (j + 1) % n) for j in range(n)] + [(n + j, n + (j - 1) % n) for j in range(n)]
    behind = [(t, f) for f, t in ahead]
    send = lambda v, pairs: lax.ppermute(v, ("walker", axis), pairs)
    return virtual, lambda v: send(v, ahead), lambda v: send(v, behind)


def half_ring_rs(x, axis, n):
    if n == 1:
        return x
    i, forward, backward = mirrored(axis, n)
    width = x.shape[1] // n
    chunk = lambda c: lax.dynamic_slice_in_dim(x, (c % n) * width, width, 1)
    up, down = n // 2, n - 1 - n // 2
    cw, ccw = chunk(i + up), chunk(i - down)
    for s in range(1, up + 1):
        cw = forward(cw)
        if s <= down:
            ccw = backward(ccw)
        if s < up:
            cw = cw + chunk(i + up - s)
        if s < down:
            ccw = ccw + chunk(i - down + s)
    if down == 0:
        return chunk(i) + cw
    return chunk(i) + cw + ccw


def half_ring_ag(x, axis, n):
    if n == 1:
        return x
    i, forward, backward = mirrored(axis, n)
    width = x.shape[1]
    up, down = n // 2, n - 1 - n // 2
    out = jnp.zeros(x.shape[:1] + (n * width,), x.dtype)
    out = lax.dynamic_update_slice_in_dim(out, x, i * width, 1)
    cw, ccw = x, x
    for s in range(1, up + 1):
        cw = forward(cw)
        out = lax.dynamic_update_slice_in_dim(out, cw, ((i - s) % n) * width, 1)
        if s <= down:
            ccw = backward(ccw)
            out = lax.dynamic_update_slice_in_dim(out, ccw, ((i + s) % n) * width, 1)
    return out


def direct_rs(x, axis, n):
    i = lax.axis_index(axis)
    width = x.shape[1] // n
    chunk = lambda c: lax.dynamic_slice_in_dim(x, (c % n) * width, width, 1)
    total = chunk(i)
    for d in SHIFTS[n]:
        total = total + lax.ppermute(chunk(i + d), axis, shift_perm(n, d))
    return total


def direct_ag(x, axis, n):
    i = lax.axis_index(axis)
    width = x.shape[1]
    out = jnp.zeros(x.shape[:1] + (n * width,), x.dtype)
    out = lax.dynamic_update_slice_in_dim(out, x, i * width, 1)
    for d in SHIFTS[n]:
        got = lax.ppermute(x, axis, shift_perm(n, d))
        out = lax.dynamic_update_slice_in_dim(out, got, ((i - d) % n) * width, 1)
    return out


SHIFTS = {2: (1,), 4: (1, -1, 2)}


def ring_allreduce(x, phases):
    for axis, n in phases:
        x = direct_rs(x, axis, n) if n in SHIFTS else half_ring_rs(x, axis, n)
    for axis, n in reversed(phases):
        x = direct_ag(x, axis, n) if n in SHIFTS else half_ring_ag(x, axis, n)
    return x


def on_device(inverse_rows, row_values, orbital_blocks, moved, accepted):
    row_count = inverse_rows.shape[0]
    block_width = row_values.shape[2]
    blocks_here = row_count // block_width
    owned_blocks = lax.axis_index(ELEC) * blocks_here + jnp.arange(blocks_here, dtype=jnp.int32)
    onehot = (orbital_blocks[:, :, None] == owned_blocks[None, None, :]).astype(jnp.float32)
    change = jnp.einsum("ksb,kst->kbt", onehot, row_values, precision=HI).reshape(MOVES, row_count)
    picked = jnp.take(inverse_rows, moved, axis=1)
    local_weights = jnp.dot(change, inverse_rows, precision=HI)
    full_weights = ring_allreduce(local_weights, PHASES)
    electrons = full_weights.shape[1]
    pick = (lax.broadcasted_iota(jnp.int32, (electrons, MOVES), 0) == moved[None, :]).astype(jnp.float32)
    intersection = jnp.dot(full_weights, pick, precision=HI)
    coupling, ratios = border(intersection, accepted)
    factor = jnp.dot(picked, coupling, precision=HI)
    new_inverse = inverse_rows - jnp.dot(factor, full_weights, precision=HI)
    return (new_inverse, ratios)


ELEC = ("x", "z", "y")
PHASES = (("z", 8), ("y", 4), ("x", 4))


def solution(mesh):
    walkers, elec = mesh.devices.shape
    torus = mesh.devices.reshape(walkers, 4, 8, elec // 32)
    mesh = Mesh(torus, ("walker",) + ELEC)
    rows = ("walker",) + ELEC
    placed = (
        P(rows, None),
        P("walker", None, None),
        P("walker", None),
        P("walker"),
        P("walker"),
    )
    return jax.shard_map(
        on_device,
        mesh=mesh,
        in_specs=placed,
        out_specs=(P(rows, None), P("walker")),
        check_vma=False,
    )
```

```python
import jax
import jax.numpy as jnp
from jax import lax
from jax.sharding import Mesh, PartitionSpec as P
from jax.experimental import pallas as pl
from jax.experimental.pallas import tpu as pltpu

MOVES = 64


HI = lax.Precision.HIGHEST


def border_step(coupling, row_vec, col_vec, accept_flag, unit_row):
    left_vec = jnp.dot(row_vec, coupling, precision=HI)
    right_vec = jnp.dot(coupling, col_vec, precision=HI)
    det_ratio = (
        1.0 + jnp.dot(row_vec, unit_row, precision=HI) - jnp.dot(left_vec, col_vec, precision=HI)
    )
    coupling = (
        coupling + accept_flag * jnp.outer(right_vec - unit_row, left_vec - unit_row) / det_ratio
    )
    return (coupling, det_ratio)


def run_border(intersection, accepted):

    def one_step(coupling, step_items):
        row_vec, col_vec, accept_flag, unit_row = step_items
        return border_step(coupling, row_vec, col_vec, accept_flag, unit_row)

    start_value = jnp.zeros((MOVES, MOVES), jnp.float32)
    step_items = (
        intersection,
        intersection.T,
        accepted.astype(jnp.float32),
        jnp.eye(MOVES, dtype=jnp.float32),
    )
    return lax.scan(one_step, start_value, step_items)


def _border_kernel(m_ref, mt_ref, acc_ref, c_ref, r_ref):
    n = m_ref.shape[0]
    lane = lax.broadcasted_iota(jnp.int32, (1, n), 1)
    sub = lax.broadcasted_iota(jnp.int32, (n, 1), 0)
    mt = mt_ref[...]
    acc = acc_ref[...]

    def step(k, carry):
        c, ratios = carry
        e_row = (lane == k).astype(jnp.float32)
        e_col = (sub == k).astype(jnp.float32)
        row_row = m_ref[pl.ds(k, 1), :]
        col_row = mt_ref[pl.ds(k, 1), :]
        row_col = jnp.sum(mt * e_row, axis=1, keepdims=True)
        left = jnp.sum(c * row_col, axis=0, keepdims=True)
        right = jnp.sum(c * col_row, axis=1, keepdims=True)
        diag = jnp.sum(row_row * e_row, axis=1, keepdims=True)
        lc = jnp.sum(left * col_row, axis=1, keepdims=True)
        ratio = 1.0 + diag - lc
        flag = jnp.sum(acc * e_row, axis=1, keepdims=True)
        c = c + flag * ((right - e_col) * (left - e_row)) / ratio
        ratios = ratios + e_row * ratio
        return c, ratios

    c0 = jnp.zeros((n, n), jnp.float32)
    r0 = jnp.zeros((1, n), jnp.float32)
    c, ratios = lax.fori_loop(0, n, step, (c0, r0), unroll=8)
    c_ref[...] = c
    r_ref[...] = ratios


def border(intersection, accepted):
    n = intersection.shape[0]
    vm = pl.BlockSpec(memory_space=pltpu.VMEM)
    c, r = pl.pallas_call(
        _border_kernel,
        out_shape=(jax.ShapeDtypeStruct((n, n), jnp.float32), jax.ShapeDtypeStruct((1, n), jnp.float32)),
        in_specs=[vm, vm, vm],
        out_specs=(vm, vm),
    )(intersection, intersection.T, accepted.astype(jnp.float32).reshape(1, n))
    return c, r.reshape(n)


def shift_perm(n, d):
    return [(j, (j + d) % n) for j in range(n)]


def half_ring_rs(x, axis, n):
    if n == 1:
        return x
    i = lax.axis_index(axis)
    width = x.shape[1] // n
    chunk = lambda c: lax.dynamic_slice_in_dim(x, (c % n) * width, width, 1)
    up, down = n // 2, n - 1 - n // 2
    cw, ccw = chunk(i + up), chunk(i - down)
    for s in range(1, up + 1):
        cw = lax.ppermute(cw, axis, shift_perm(n, 1))
        if s <= down:
            ccw = lax.ppermute(ccw, axis, shift_perm(n, -1))
        if s < up:
            cw = cw + chunk(i + up - s)
        if s < down:
            ccw = ccw + chunk(i - down + s)
    if down == 0:
        return chunk(i) + cw
    return chunk(i) + cw + ccw


def half_ring_ag(x, axis, n):
    if n == 1:
        return x
    i = lax.axis_index(axis)
    width = x.shape[1]
    up, down = n // 2, n - 1 - n // 2
    out = jnp.zeros(x.shape[:1] + (n * width,), x.dtype)
    out = lax.dynamic_update_slice_in_dim(out, x, i * width, 1)
    cw, ccw = x, x
    for s in range(1, up + 1):
        cw = lax.ppermute(cw, axis, shift_perm(n, 1))
        out = lax.dynamic_update_slice_in_dim(out, cw, ((i - s) % n) * width, 1)
        if s <= down:
            ccw = lax.ppermute(ccw, axis, shift_perm(n, -1))
            out = lax.dynamic_update_slice_in_dim(out, ccw, ((i + s) % n) * width, 1)
    return out

def direct_rs(x, axis, n):
    i = lax.axis_index(axis)
    width = x.shape[1] // n
    chunk = lambda c: lax.dynamic_slice_in_dim(x, (c % n) * width, width, 1)
    total = chunk(i)
    for d in SHIFTS[n]:
        total = total + lax.ppermute(chunk(i + d), axis, shift_perm(n, d))
    return total


def direct_ag(x, axis, n):
    i = lax.axis_index(axis)
    width = x.shape[1]
    out = jnp.zeros(x.shape[:1] + (n * width,), x.dtype)
    out = lax.dynamic_update_slice_in_dim(out, x, i * width, 1)
    for d in SHIFTS[n]:
        got = lax.ppermute(x, axis, shift_perm(n, d))
        out = lax.dynamic_update_slice_in_dim(out, got, ((i - d) % n) * width, 1)
    return out


SHIFTS = {2: (1,), 4: (2, 1, -1)}


def ring_allreduce(x, phases):
    for axis, n in phases:
        x = direct_rs(x, axis, n) if n in SHIFTS else half_ring_rs(x, axis, n)
    for axis, n in reversed(phases):
        x = direct_ag(x, axis, n) if n in SHIFTS else half_ring_ag(x, axis, n)
    return x


def on_device(inverse_rows, row_values, orbital_blocks, moved, accepted):
    row_count = inverse_rows.shape[0]
    block_width = row_values.shape[2]
    blocks_here = row_count // block_width
    owned_blocks = lax.axis_index(ELEC) * blocks_here + jnp.arange(blocks_here, dtype=jnp.int32)
    onehot = (orbital_blocks[:, :, None] == owned_blocks[None, None, :]).astype(jnp.float32)
    change = jnp.einsum("ksb,kst->kbt", onehot, row_values, precision=HI).reshape(MOVES, row_count)
    picked = jnp.take(inverse_rows, moved, axis=1)
    local_weights = jnp.dot(change, inverse_rows, precision=HI)
    full_weights = ring_allreduce(local_weights, PHASES)
    electrons = full_weights.shape[1]
    pick = (lax.broadcasted_iota(jnp.int32, (electrons, MOVES), 0) == moved[None, :]).astype(jnp.float32)
    intersection = jnp.dot(full_weights, pick, precision=HI)
    coupling, ratios = border(intersection, accepted)
    factor = jnp.dot(picked, coupling, precision=HI)
    new_inverse = inverse_rows - jnp.dot(factor, full_weights, precision=HI)
    return (new_inverse, ratios)


ELEC = ("x", "z", "y")
PHASES = (("z", 8), ("y", 4), ("x", 4))


def solution(mesh):
    walkers, elec = mesh.devices.shape
    torus = mesh.devices.reshape(walkers, 4, 8, elec // 32)
    mesh = Mesh(torus, ("walker",) + ELEC)
    rows = ("walker",) + ELEC
    placed = (
        P(rows, None),
        P("walker", None, None),
        P("walker", None),
        P("walker"),
        P("walker"),
    )
    return jax.shard_map(
        on_device,
        mesh=mesh,
        in_specs=placed,
        out_specs=(P(rows, None), P("walker")),
        check_vma=False,
    )
```

```python
import jax
import jax.numpy as jnp
from jax import lax
from jax.sharding import Mesh, PartitionSpec as P
from jax.experimental import pallas as pl
from jax.experimental.pallas import tpu as pltpu

MOVES = 64


HI = lax.Precision.HIGHEST


def border_step(coupling, row_vec, col_vec, accept_flag, unit_row):
    left_vec = jnp.dot(row_vec, coupling, precision=HI)
    right_vec = jnp.dot(coupling, col_vec, precision=HI)
    det_ratio = (
        1.0 + jnp.dot(row_vec, unit_row, precision=HI) - jnp.dot(left_vec, col_vec, precision=HI)
    )
    coupling = (
        coupling + accept_flag * jnp.outer(right_vec - unit_row, left_vec - unit_row) / det_ratio
    )
    return (coupling, det_ratio)


def run_border(intersection, accepted):

    def one_step(coupling, step_items):
        row_vec, col_vec, accept_flag, unit_row = step_items
        return border_step(coupling, row_vec, col_vec, accept_flag, unit_row)

    start_value = jnp.zeros((MOVES, MOVES), jnp.float32)
    step_items = (
        intersection,
        intersection.T,
        accepted.astype(jnp.float32),
        jnp.eye(MOVES, dtype=jnp.float32),
    )
    return lax.scan(one_step, start_value, step_items)


def _border_kernel(m_ref, mt_ref, acc_ref, c_ref, r_ref):
    n = m_ref.shape[0]
    lane = lax.broadcasted_iota(jnp.int32, (1, n), 1)
    sub = lax.broadcasted_iota(jnp.int32, (n, 1), 0)
    mt = mt_ref[...]
    acc = acc_ref[...]

    def step(k, carry):
        c, ratios = carry
        e_row = (lane == k).astype(jnp.float32)
        e_col = (sub == k).astype(jnp.float32)
        row_row = m_ref[pl.ds(k, 1), :]
        col_row = mt_ref[pl.ds(k, 1), :]
        row_col = jnp.sum(mt * e_row, axis=1, keepdims=True)
        left = jnp.sum(c * row_col, axis=0, keepdims=True)
        right = jnp.sum(c * col_row, axis=1, keepdims=True)
        diag = jnp.sum(row_row * e_row, axis=1, keepdims=True)
        lc = jnp.sum(left * col_row, axis=1, keepdims=True)
        ratio = 1.0 + diag - lc
        flag = jnp.sum(acc * e_row, axis=1, keepdims=True)
        c = c + flag * ((right - e_col) * (left - e_row)) / ratio
        ratios = ratios + e_row * ratio
        return c, ratios

    c0 = jnp.zeros((n, n), jnp.float32)
    r0 = jnp.zeros((1, n), jnp.float32)
    c, ratios = lax.fori_loop(0, n, step, (c0, r0), unroll=8)
    c_ref[...] = c
    r_ref[...] = ratios


def border(intersection, accepted):
    n = intersection.shape[0]
    vm = pl.BlockSpec(memory_space=pltpu.VMEM)
    c, r = pl.pallas_call(
        _border_kernel,
        out_shape=(jax.ShapeDtypeStruct((n, n), jnp.float32), jax.ShapeDtypeStruct((1, n), jnp.float32)),
        in_specs=[vm, vm, vm],
        out_specs=(vm, vm),
    )(intersection, intersection.T, accepted.astype(jnp.float32).reshape(1, n))
    return c, r.reshape(n)


def shift_perm(n, d):
    return [(j, (j + d) % n) for j in range(n)]


def half_ring_rs(x, axis, n, chunk=None):
    i = lax.axis_index(axis)
    if chunk is None:
        width = x.shape[1] // n
        chunk = lambda c: lax.dynamic_slice_in_dim(x, (c % n) * width, width, 1)
    up, down = n // 2, n - 1 - n // 2
    cw, ccw = chunk(i + up), chunk(i - down)
    for s in range(1, up + 1):
        cw = lax.ppermute(cw, axis, shift_perm(n, 1))
        if s <= down:
            ccw = lax.ppermute(ccw, axis, shift_perm(n, -1))
        if s < up:
            cw = cw + chunk(i + up - s)
        if s < down:
            ccw = ccw + chunk(i - down + s)
    if down == 0:
        return chunk(i) + cw
    return chunk(i) + cw + ccw


def half_ring_ag(x, axis, n):
    if n == 1:
        return x
    i = lax.axis_index(axis)
    width = x.shape[1]
    up, down = n // 2, n - 1 - n // 2
    out = jnp.zeros(x.shape[:1] + (n * width,), x.dtype)
    out = lax.dynamic_update_slice_in_dim(out, x, i * width, 1)
    cw, ccw = x, x
    for s in range(1, up + 1):
        cw = lax.ppermute(cw, axis, shift_perm(n, 1))
        out = lax.dynamic_update_slice_in_dim(out, cw, ((i - s) % n) * width, 1)
        if s <= down:
            ccw = lax.ppermute(ccw, axis, shift_perm(n, -1))
            out = lax.dynamic_update_slice_in_dim(out, ccw, ((i + s) % n) * width, 1)
    return out

def direct_rs(x, axis, n):
    i = lax.axis_index(axis)
    width = x.shape[1] // n
    chunk = lambda c: lax.dynamic_slice_in_dim(x, (c % n) * width, width, 1)
    total = chunk(i)
    for d in SHIFTS[n]:
        total = total + lax.ppermute(chunk(i + d), axis, shift_perm(n, d))
    return total


def direct_ag(x, axis, n):
    i = lax.axis_index(axis)
    width = x.shape[1]
    out = jnp.zeros(x.shape[:1] + (n * width,), x.dtype)
    out = lax.dynamic_update_slice_in_dim(out, x, i * width, 1)
    for d in SHIFTS[n]:
        got = lax.ppermute(x, axis, shift_perm(n, d))
        out = lax.dynamic_update_slice_in_dim(out, got, ((i - d) % n) * width, 1)
    return out


SHIFTS = {2: (1,), 4: (2, 1, -1)}


def ring_allreduce(make_chunk, phases):
    axis, n = phases[0]
    x = half_ring_rs(None, axis, n, lambda c: make_chunk(c % n, n))
    for axis, n in phases[1:]:
        x = direct_rs(x, axis, n) if n in SHIFTS else half_ring_rs(x, axis, n)
    for axis, n in reversed(phases):
        x = direct_ag(x, axis, n) if n in SHIFTS else half_ring_ag(x, axis, n)
    return x


def on_device(inverse_rows, row_values, orbital_blocks, moved, accepted):
    row_count = inverse_rows.shape[0]
    block_width = row_values.shape[2]
    blocks_here = row_count // block_width
    owned_blocks = lax.axis_index(ELEC) * blocks_here + jnp.arange(blocks_here, dtype=jnp.int32)
    onehot = (orbital_blocks[:, :, None] == owned_blocks[None, None, :]).astype(jnp.float32)
    change = jnp.einsum("ksb,kst->kbt", onehot, row_values, precision=HI).reshape(MOVES, row_count)
    picked = jnp.take(inverse_rows, moved, axis=1)
    electrons = inverse_rows.shape[1]

    def local_chunk(c, n):
        width = electrons // n
        return jnp.dot(change, lax.dynamic_slice_in_dim(inverse_rows, c * width, width, 1), precision=HI)

    full_weights = ring_allreduce(local_chunk, PHASES)
    pick = (lax.broadcasted_iota(jnp.int32, (electrons, MOVES), 0) == moved[None, :]).astype(jnp.float32)
    intersection = jnp.dot(full_weights, pick, precision=HI)
    coupling, ratios = border(intersection, accepted)
    factor = jnp.dot(picked, coupling, precision=HI)
    new_inverse = inverse_rows - jnp.dot(factor, full_weights, precision=HI)
    return (new_inverse, ratios)


ELEC = ("x", "z", "y")
PHASES = (("z", 8), ("y", 4), ("x", 4))


def solution(mesh):
    walkers, elec = mesh.devices.shape
    torus = mesh.devices.reshape(walkers, 4, 8, elec // 32)
    mesh = Mesh(torus, ("walker",) + ELEC)
    rows = ("walker",) + ELEC
    placed = (
        P(rows, None),
        P("walker", None, None),
        P("walker", None),
        P("walker"),
        P("walker"),
    )
    return jax.shard_map(
        on_device,
        mesh=mesh,
        in_specs=placed,
        out_specs=(P(rows, None), P("walker")),
        check_vma=False,
    )
```

```python
import jax
import jax.numpy as jnp
from jax import lax
from jax.sharding import Mesh, PartitionSpec as P
from jax.experimental import pallas as pl
from jax.experimental.pallas import tpu as pltpu

MOVES = 64


HI = lax.Precision.HIGHEST


def border_step(coupling, row_vec, col_vec, accept_flag, unit_row):
    left_vec = jnp.dot(row_vec, coupling, precision=HI)
    right_vec = jnp.dot(coupling, col_vec, precision=HI)
    det_ratio = (
        1.0 + jnp.dot(row_vec, unit_row, precision=HI) - jnp.dot(left_vec, col_vec, precision=HI)
    )
    coupling = (
        coupling + accept_flag * jnp.outer(right_vec - unit_row, left_vec - unit_row) / det_ratio
    )
    return (coupling, det_ratio)


def run_border(intersection, accepted):

    def one_step(coupling, step_items):
        row_vec, col_vec, accept_flag, unit_row = step_items
        return border_step(coupling, row_vec, col_vec, accept_flag, unit_row)

    start_value = jnp.zeros((MOVES, MOVES), jnp.float32)
    step_items = (
        intersection,
        intersection.T,
        accepted.astype(jnp.float32),
        jnp.eye(MOVES, dtype=jnp.float32),
    )
    return lax.scan(one_step, start_value, step_items)


def _border_kernel(m_ref, mt_ref, acc_ref, c_ref, r_ref):
    n = m_ref.shape[0]
    lane = lax.broadcasted_iota(jnp.int32, (1, n), 1)
    sub = lax.broadcasted_iota(jnp.int32, (n, 1), 0)
    mt = mt_ref[...]
    acc = acc_ref[...]

    def step(k, carry):
        c, ratios = carry
        e_row = (lane == k).astype(jnp.float32)
        e_col = (sub == k).astype(jnp.float32)
        row_row = m_ref[pl.ds(k, 1), :]
        col_row = mt_ref[pl.ds(k, 1), :]
        row_col = jnp.sum(mt * e_row, axis=1, keepdims=True)
        left = jnp.sum(c * row_col, axis=0, keepdims=True)
        right = jnp.sum(c * col_row, axis=1, keepdims=True)
        diag = jnp.sum(row_row * e_row, axis=1, keepdims=True)
        lc = jnp.sum(left * col_row, axis=1, keepdims=True)
        ratio = 1.0 + diag - lc
        flag = jnp.sum(acc * e_row, axis=1, keepdims=True)
        c = c + flag * ((right - e_col) * (left - e_row)) / ratio
        ratios = ratios + e_row * ratio
        return c, ratios

    c0 = jnp.zeros((n, n), jnp.float32)
    r0 = jnp.zeros((1, n), jnp.float32)
    c, ratios = lax.fori_loop(0, n, step, (c0, r0), unroll=8)
    c_ref[...] = c
    r_ref[...] = ratios


def border(intersection, accepted):
    n = intersection.shape[0]
    vm = pl.BlockSpec(memory_space=pltpu.VMEM)
    c, r = pl.pallas_call(
        _border_kernel,
        out_shape=(jax.ShapeDtypeStruct((n, n), jnp.float32), jax.ShapeDtypeStruct((1, n), jnp.float32)),
        in_specs=[vm, vm, vm],
        out_specs=(vm, vm),
    )(intersection, intersection.T, accepted.astype(jnp.float32).reshape(1, n))
    return c, r.reshape(n)


def shift_perm(n, d):
    return [(j, (j + d) % n) for j in range(n)]


def half_ring_rs(x, axis, n, chunk=None):
    i = lax.axis_index(axis)
    if chunk is None:
        width = x.shape[1] // n
        chunk = lambda c: lax.dynamic_slice_in_dim(x, (c % n) * width, width, 1)
    up, down = n // 2, n - 1 - n // 2
    cw, ccw = chunk(i + up), chunk(i - down)
    if x is not None:
        width = x.shape[1] // n
        chunk = lambda c: lax.dynamic_slice_in_dim(x, (c % n) * width, width, 1)
    for s in range(1, up + 1):
        cw = lax.ppermute(cw, axis, shift_perm(n, 1))
        if s <= down:
            ccw = lax.ppermute(ccw, axis, shift_perm(n, -1))
        if s < up:
            cw = cw + chunk(i + up - s)
        if s < down:
            ccw = ccw + chunk(i - down + s)
    if down == 0:
        return chunk(i) + cw
    return chunk(i) + cw + ccw


def half_ring_ag(x, axis, n):
    if n == 1:
        return x
    i = lax.axis_index(axis)
    width = x.shape[1]
    up, down = n // 2, n - 1 - n // 2
    out = jnp.zeros(x.shape[:1] + (n * width,), x.dtype)
    out = lax.dynamic_update_slice_in_dim(out, x, i * width, 1)
    cw, ccw = x, x
    for s in range(1, up + 1):
        cw = lax.ppermute(cw, axis, shift_perm(n, 1))
        out = lax.dynamic_update_slice_in_dim(out, cw, ((i - s) % n) * width, 1)
        if s <= down:
            ccw = lax.ppermute(ccw, axis, shift_perm(n, -1))
            out = lax.dynamic_update_slice_in_dim(out, ccw, ((i + s) % n) * width, 1)
    return out

def direct_rs(x, axis, n):
    i = lax.axis_index(axis)
    width = x.shape[1] // n
    chunk = lambda c: lax.dynamic_slice_in_dim(x, (c % n) * width, width, 1)
    total = chunk(i)
    for d in SHIFTS[n]:
        total = total + lax.ppermute(chunk(i + d), axis, shift_perm(n, d))
    return total


def direct_ag(x, axis, n):
    i = lax.axis_index(axis)
    width = x.shape[1]
    out = jnp.zeros(x.shape[:1] + (n * width,), x.dtype)
    out = lax.dynamic_update_slice_in_dim(out, x, i * width, 1)
    for d in SHIFTS[n]:
        got = lax.ppermute(x, axis, shift_perm(n, d))
        out = lax.dynamic_update_slice_in_dim(out, got, ((i - d) % n) * width, 1)
    return out


SHIFTS = {2: (1,), 4: (2, 1, -1)}


def ring_allreduce(make_chunk, phases):
    axis, n = phases[0]
    x = half_ring_rs(make_chunk(None, n), axis, n, lambda c: make_chunk(c % n, n))
    for axis, n in phases[1:]:
        x = direct_rs(x, axis, n) if n in SHIFTS else half_ring_rs(x, axis, n)
    for axis, n in reversed(phases):
        x = direct_ag(x, axis, n) if n in SHIFTS else half_ring_ag(x, axis, n)
    return x


def on_device(inverse_rows, row_values, orbital_blocks, moved, accepted):
    row_count = inverse_rows.shape[0]
    block_width = row_values.shape[2]
    blocks_here = row_count // block_width
    owned_blocks = lax.axis_index(ELEC) * blocks_here + jnp.arange(blocks_here, dtype=jnp.int32)
    onehot = (orbital_blocks[:, :, None] == owned_blocks[None, None, :]).astype(jnp.float32)
    change = jnp.einsum("ksb,kst->kbt", onehot, row_values, precision=HI).reshape(MOVES, row_count)
    picked = jnp.take(inverse_rows, moved, axis=1)
    electrons = inverse_rows.shape[1]

    def local_chunk(c, n):
        if c is None:
            return jnp.dot(change, inverse_rows, precision=HI)
        width = electrons // n
        return jnp.dot(change, lax.dynamic_slice_in_dim(inverse_rows, c * width, width, 1), precision=HI)

    full_weights = ring_allreduce(local_chunk, PHASES)
    pick = (lax.broadcasted_iota(jnp.int32, (electrons, MOVES), 0) == moved[None, :]).astype(jnp.float32)
    intersection = jnp.dot(full_weights, pick, precision=HI)
    coupling, ratios = border(intersection, accepted)
    factor = jnp.dot(picked, coupling, precision=HI)
    new_inverse = inverse_rows - jnp.dot(factor, full_weights, precision=HI)
    return (new_inverse, ratios)


ELEC = ("x", "z", "y")
PHASES = (("z", 8), ("y", 4), ("x", 4))


def solution(mesh):
    walkers, elec = mesh.devices.shape
    torus = mesh.devices.reshape(walkers, 4, 8, elec // 32)
    mesh = Mesh(torus, ("walker",) + ELEC)
    rows = ("walker",) + ELEC
    placed = (
        P(rows, None),
        P("walker", None, None),
        P("walker", None),
        P("walker"),
        P("walker"),
    )
    return jax.shard_map(
        on_device,
        mesh=mesh,
        in_specs=placed,
        out_specs=(P(rows, None), P("walker")),
        check_vma=False,
    )
```

```python
import jax
import jax.numpy as jnp
from jax import lax
from jax.sharding import Mesh, PartitionSpec as P
from jax.experimental import pallas as pl
from jax.experimental.pallas import tpu as pltpu

MOVES = 64


HI = lax.Precision.HIGHEST


def border_step(coupling, row_vec, col_vec, accept_flag, unit_row):
    left_vec = jnp.dot(row_vec, coupling, precision=HI)
    right_vec = jnp.dot(coupling, col_vec, precision=HI)
    det_ratio = (
        1.0 + jnp.dot(row_vec, unit_row, precision=HI) - jnp.dot(left_vec, col_vec, precision=HI)
    )
    coupling = (
        coupling + accept_flag * jnp.outer(right_vec - unit_row, left_vec - unit_row) / det_ratio
    )
    return (coupling, det_ratio)


def run_border(intersection, accepted):

    def one_step(coupling, step_items):
        row_vec, col_vec, accept_flag, unit_row = step_items
        return border_step(coupling, row_vec, col_vec, accept_flag, unit_row)

    start_value = jnp.zeros((MOVES, MOVES), jnp.float32)
    step_items = (
        intersection,
        intersection.T,
        accepted.astype(jnp.float32),
        jnp.eye(MOVES, dtype=jnp.float32),
    )
    return lax.scan(one_step, start_value, step_items)


def _border_kernel(m_ref, acc_ref, c_ref, r_ref, mt_ref):
    n = m_ref.shape[0]
    lane = lax.broadcasted_iota(jnp.int32, (1, n), 1)
    sub = lax.broadcasted_iota(jnp.int32, (n, 1), 0)
    mt = jnp.transpose(m_ref[...])
    mt_ref[...] = mt
    acc = acc_ref[...]

    def step(k, carry):
        c, ratios = carry
        e_row = (lane == k).astype(jnp.float32)
        e_col = (sub == k).astype(jnp.float32)
        row_row = m_ref[pl.ds(k, 1), :]
        col_row = mt_ref[pl.ds(k, 1), :]
        row_col = jnp.sum(mt * e_row, axis=1, keepdims=True)
        left = jnp.sum(c * row_col, axis=0, keepdims=True)
        right = jnp.sum(c * col_row, axis=1, keepdims=True)
        diag = jnp.sum(row_row * e_row, axis=1, keepdims=True)
        lc = jnp.sum(left * col_row, axis=1, keepdims=True)
        ratio = 1.0 + diag - lc
        flag = jnp.sum(acc * e_row, axis=1, keepdims=True)
        c = c + flag * ((right - e_col) * (left - e_row)) / ratio
        ratios = ratios + e_row * ratio
        return c, ratios

    c0 = jnp.zeros((n, n), jnp.float32)
    r0 = jnp.zeros((1, n), jnp.float32)
    c, ratios = lax.fori_loop(0, n, step, (c0, r0), unroll=8)
    c_ref[...] = c
    r_ref[...] = ratios


def border(intersection, accepted):
    n = intersection.shape[0]
    vm = pl.BlockSpec(memory_space=pltpu.VMEM)
    c, r = pl.pallas_call(
        _border_kernel,
        out_shape=(jax.ShapeDtypeStruct((n, n), jnp.float32), jax.ShapeDtypeStruct((1, n), jnp.float32)),
        in_specs=[vm, vm],
        scratch_shapes=[pltpu.VMEM((n, n), jnp.float32)],
        out_specs=(vm, vm),
    )(intersection, accepted.astype(jnp.float32).reshape(1, n))
    return c, r.reshape(n)


def shift_perm(n, d):
    return [(j, (j + d) % n) for j in range(n)]


def half_ring_rs(x, axis, n, chunk=None):
    i = lax.axis_index(axis)
    if chunk is None:
        width = x.shape[1] // n
        chunk = lambda c: lax.dynamic_slice_in_dim(x, (c % n) * width, width, 1)
    up, down = n // 2, n - 1 - n // 2
    cw, ccw = chunk(i + up), chunk(i - down)
    if x is not None:
        width = x.shape[1] // n
        chunk = lambda c: lax.dynamic_slice_in_dim(x, (c % n) * width, width, 1)
    for s in range(1, up + 1):
        cw = lax.ppermute(cw, axis, shift_perm(n, 1))
        if s <= down:
            ccw = lax.ppermute(ccw, axis, shift_perm(n, -1))
        if s < up:
            cw = cw + chunk(i + up - s)
        if s < down:
            ccw = ccw + chunk(i - down + s)
    if down == 0:
        return chunk(i) + cw
    return chunk(i) + cw + ccw


def half_ring_ag(x, axis, n):
    if n == 1:
        return x
    i = lax.axis_index(axis)
    width = x.shape[1]
    up, down = n // 2, n - 1 - n // 2
    out = jnp.zeros(x.shape[:1] + (n * width,), x.dtype)
    out = lax.dynamic_update_slice_in_dim(out, x, i * width, 1)
    cw, ccw = x, x
    for s in range(1, up + 1):
        cw = lax.ppermute(cw, axis, shift_perm(n, 1))
        out = lax.dynamic_update_slice_in_dim(out, cw, ((i - s) % n) * width, 1)
        if s <= down:
            ccw = lax.ppermute(ccw, axis, shift_perm(n, -1))
            out = lax.dynamic_update_slice_in_dim(out, ccw, ((i + s) % n) * width, 1)
    return out

def direct_rs(x, axis, n):
    i = lax.axis_index(axis)
    width = x.shape[1] // n
    chunk = lambda c: lax.dynamic_slice_in_dim(x, (c % n) * width, width, 1)
    total = chunk(i)
    for d in SHIFTS[n]:
        total = total + lax.ppermute(chunk(i + d), axis, shift_perm(n, d))
    return total


def direct_ag(x, axis, n):
    i = lax.axis_index(axis)
    width = x.shape[1]
    out = jnp.zeros(x.shape[:1] + (n * width,), x.dtype)
    out = lax.dynamic_update_slice_in_dim(out, x, i * width, 1)
    for d in SHIFTS[n]:
        got = lax.ppermute(x, axis, shift_perm(n, d))
        out = lax.dynamic_update_slice_in_dim(out, got, ((i - d) % n) * width, 1)
    return out


SHIFTS = {2: (1,), 4: (2, 1, -1)}


def ring_allreduce(make_chunk, phases):
    axis, n = phases[0]
    x = half_ring_rs(make_chunk(None, n), axis, n, lambda c: make_chunk(c % n, n))
    for axis, n in phases[1:]:
        x = direct_rs(x, axis, n) if n in SHIFTS else half_ring_rs(x, axis, n)
    for axis, n in reversed(phases):
        x = direct_ag(x, axis, n) if n in SHIFTS else half_ring_ag(x, axis, n)
    return x


def on_device(inverse_rows, row_values, orbital_blocks, moved, accepted):
    row_count = inverse_rows.shape[0]
    block_width = row_values.shape[2]
    blocks_here = row_count // block_width
    owned_blocks = lax.axis_index(ELEC) * blocks_here + jnp.arange(blocks_here, dtype=jnp.int32)
    onehot = (orbital_blocks[:, :, None] == owned_blocks[None, None, :]).astype(jnp.float32)
    change = jnp.einsum("ksb,kst->kbt", onehot, row_values, precision=HI).reshape(MOVES, row_count)
    picked = jnp.take(inverse_rows, moved, axis=1)
    electrons = inverse_rows.shape[1]

    def local_chunk(c, n):
        if c is None:
            return jnp.dot(change, inverse_rows, precision=HI)
        width = electrons // n
        return jnp.dot(change, lax.dynamic_slice_in_dim(inverse_rows, c * width, width, 1), precision=HI)

    full_weights = ring_allreduce(local_chunk, PHASES)
    pick = (lax.broadcasted_iota(jnp.int32, (electrons, MOVES), 0) == moved[None, :]).astype(jnp.float32)
    intersection = jnp.dot(full_weights, pick, precision=HI)
    coupling, ratios = border(intersection, accepted)
    factor = jnp.dot(picked, coupling, precision=HI)
    new_inverse = inverse_rows - jnp.dot(factor, full_weights, precision=HI)
    return (new_inverse, ratios)


ELEC = ("x", "z", "y")
PHASES = (("z", 8), ("y", 4), ("x", 4))


def solution(mesh):
    walkers, elec = mesh.devices.shape
    torus = mesh.devices.reshape(walkers, 4, 8, elec // 32)
    mesh = Mesh(torus, ("walker",) + ELEC)
    rows = ("walker",) + ELEC
    placed = (
        P(rows, None),
        P("walker", None, None),
        P("walker", None),
        P("walker"),
        P("walker"),
    )
    return jax.shard_map(
        on_device,
        mesh=mesh,
        in_specs=placed,
        out_specs=(P(rows, None), P("walker")),
        check_vma=False,
    )
```
